32 devices in a mesh: tok: 4 (over y, x), voc: 8 (over z, core).
Axes of the slice: x: 2, y: 2, z: 4, core: 2. Of those that a mesh axis runs over, the one named last changes fastest.
Arguments:
- hidden: bfloat16 [8192, 2048], P(('tok', 'voc')), as said below
- gain: bfloat16 [2048], replicated, may hold values from 0.5 to 1.5
- head: bfloat16 [2048, 50304], P(None, 'voc')
- targets: int32 [8192], replicated, may hold values from 0 to 50303
- lengths: int32 [8], replicated, may hold values from 1 to 1024, 5120 in all
- perm: int32 [8], replicated, may hold values from 0 to 7, each once
Outputs:
- logprob: float32 [5120], P(('tok', 'voc'))
- entropy: float32 [5120], P(('tok', 'voc'))
The draws below stay inside these ranges and needn't reach their ends.
Inputs may be any that keep to these rules, and one draw needn't show every extreme that they name: Each request has at least one token and the longest has exactly 1024; the lengths sum to 5120. `perm`: each request is held by exactly one slot. `hidden`: rows past a request's length in its slot are not read by any output.
All inputs are finite; a program needn't handle non-finite values.
Results may differ from the reference program's by a relative error of at most 0.0024.
Values may be sent and summed in bfloat16 or wider, within the bound.
No kernel may reach another device: no remote copies, remote signals or barrier semaphores. Data moves between devices by JAX's collectives and lax.ppermute only.
A program may use at most 256 MiB of HBM per device.

```python
import math
import jax
import jax.numpy as jnp
import numpy as np
from jax import lax

D = 2048
VOCAB = 50304
MAXLEN = 1024
NREQ = 8
TOTAL = 5120


def head_matrix(key):
    factor = max(1.0, 48.0 / D ** 0.5)
    return jax.random.normal(jax.random.fold_in(key, 11), (D, VOCAB), jnp.float32) * (4.0 * factor / D ** 0.5)


def draw_head(key, part):
    return head_matrix(key).astype(jnp.bfloat16)


def draw_hidden(key, part):
    count = NREQ * MAXLEN
    noise_key = jax.random.fold_in(key, 23)
    base = jax.random.normal(noise_key, (count, D), jnp.float32)
    weights = head_matrix(key)
    rows = jnp.arange(count, dtype=jnp.int32)
    first = (rows * 7919 + 13) % VOCAB
    second = (first + 1 + rows * 31 % (VOCAB - 1)) % VOCAB
    aligned = jnp.take(weights, first, axis=1).T + 0.985 * jnp.take(weights, second, axis=1).T
    strength = (rows // 61 % 3).astype(jnp.float32) * 0.3
    noise = jax.random.normal(jax.random.fold_in(key, 31), (count, D), jnp.float32)
    mixed = aligned + strength[:, None] * noise * (4.0 * max(1.0, 48.0 / D ** 0.5) / D ** 0.5)
    chosen = rows % 61 == 0
    values = jnp.where(chosen[:, None], mixed, base)
    return values.astype(jnp.bfloat16)


def set_ends(drawn, own_key, smallest, high):
    index_at = [jax.random.randint(jax.random.fold_in(own_key, axis), (), 0, length) for axis, length in enumerate(drawn.shape)]
    longest = drawn.shape.index(max(drawn.shape))
    beside = index_at[:longest] + [(index_at[longest] + 1) % drawn.shape[longest]] + index_at[longest + 1:]
    return drawn.at[tuple(index_at)].set(smallest).at[tuple(beside)].set(high)


def length_profile(count, total, limit, slope):
    weights = [(1 << 20) // math.isqrt(standing ** slope) + 1 for standing in range(2, count + 1)]
    rest, given = total - limit - (count - 1), [1] * (count - 1)
    while rest > 0:
        free = [i for i in range(count - 1) if given[i] < limit]
        whole, budget = sum([weights[i] for i in free]), rest
        for i in free:
            extra = min(limit - given[i], max(1, budget * weights[i] // whole), rest)
            given[i] = given[i] + extra
            rest = rest - extra
    return np.array([limit] + given)


def uneven_parts(key, amount, total, most, slope):
    if amount == 2:
        one = jax.random.randint(key, (), max(1, total - most), min(most, total - 1) + 1)
        return jnp.stack([one, total - one])
    sizes = jnp.asarray(length_profile(amount, total, most, slope), jnp.int32)
    couples = (amount - 1) // 2
    source_of, receiver = sizes[1:1 + 2 * couples:2], sizes[2:2 + 2 * couples:2]
    margin = jnp.minimum(source_of - 1, most - receiver)
    moved = jax.random.randint(jax.random.fold_in(key, 1), (couples,), 0, 1 << 20) % (margin + 1)
    sizes = sizes.at[1:1 + 2 * couples:2].set(source_of - moved).at[2:2 + 2 * couples:2].set(receiver + moved)
    return sizes[jax.random.permutation(jax.random.fold_in(key, 2), amount)]


def setup_inputs(seed: int = 0) -> dict:
    key_of = jax.random.split(jax.random.key(seed), 7)
    return {
        "hidden": draw_hidden(jax.random.fold_in(key_of[6], 71), 0),
        "gain": jnp.clip(1.0 + 0.1 * jax.random.normal(key_of[1], (D,), jnp.float32), 0.5, 1.5).astype(jnp.bfloat16),
        "head": draw_head(jax.random.fold_in(key_of[6], 71), 0),
        "targets": set_ends(jax.random.randint(key_of[3], (NREQ * MAXLEN,), 0, VOCAB), jax.random.fold_in(key_of[3], 1), 0, VOCAB - 1).astype(jnp.int32),
        "lengths": uneven_parts(key_of[4], NREQ, TOTAL, MAXLEN, 2).astype(jnp.int32),
        "perm": jax.random.permutation(key_of[5], NREQ).astype(jnp.int32),
    }


def slot_rows(positions, lengths, perm):
    count = lengths.shape[0]
    ident = jnp.arange(count, dtype=jnp.int32)
    starts = (jnp.cumsum(lengths) - lengths).astype(jnp.int32)
    request = (lax.optimization_barrier(jnp.sum((positions[:, None] >= starts[None, :]).astype(jnp.int32), axis=1)) - 1).astype(jnp.int32)
    start_of = lax.optimization_barrier(jnp.sum(jnp.where(ident[None, :] == request[:, None], starts[None, :], 0), axis=1)).astype(jnp.int32)
    slot_of = lax.optimization_barrier(jnp.sum(jnp.where(perm[None, :] == request[:, None], ident[None, :], 0), axis=1)).astype(jnp.int32)
    return (slot_of * MAXLEN + positions - start_of).astype(jnp.int32)

def reference(hidden, gain, head, targets, lengths, perm):
    values = hidden.astype(jnp.float32)
    scale = lax.rsqrt(lax.optimization_barrier(jnp.mean(values * values, axis=1, keepdims=True)) + 1e-06)
    normed = (values * scale * gain.astype(jnp.float32)[None, :]).astype(jnp.bfloat16)
    weights = head.astype(jnp.float32)
    blocks = normed.shape[0] // 512
    columns = jnp.arange(weights.shape[1], dtype=jnp.int32)

    def one_block(index):
        rows = lax.dynamic_slice_in_dim(normed, index * 512, 512, 0).astype(jnp.float32)
        wanted = lax.dynamic_slice_in_dim(targets, index * 512, 512, 0)
        logits = jnp.dot(rows, weights)
        peak = lax.optimization_barrier(jnp.max(logits, axis=1))
        expo = jnp.exp(logits - peak[:, None])
        total = lax.optimization_barrier(jnp.sum(expo, axis=1))
        moment = lax.optimization_barrier(jnp.sum(expo * logits, axis=1))
        picked = lax.optimization_barrier(jnp.sum(jnp.where(columns[None, :] == wanted[:, None], logits, 0.0), axis=1))
        lse = peak + jnp.log(total)
        return jnp.stack([picked - lse, lse - moment / total], axis=0)
    stats = lax.map(one_block, jnp.arange(blocks, dtype=jnp.int32))
    row_logprob = stats[:, 0, :].reshape(-1)
    row_entropy = stats[:, 1, :].reshape(-1)
    positions = jnp.arange(TOTAL, dtype=jnp.int32)
    rows = slot_rows(positions, lengths, perm)
    return (row_logprob[rows], row_entropy[rows])
```

```python
import jax
import jax.numpy as jnp
from jax import lax
from jax.sharding import PartitionSpec as P

MAXLEN = 1024
CHUNKS = 4


def slot_rows(positions, lengths, perm):
    count = lengths.shape[0]
    ident = jnp.arange(count, dtype=jnp.int32)
    starts = jnp.cumsum(lengths) - lengths
    request = jnp.sum((positions[:, None] >= starts[None, :]).astype(jnp.int32), axis=1) - 1
    start_of = jnp.sum(jnp.where(ident[None, :] == request[:, None], starts[None, :], 0), axis=1)
    slot_of = jnp.sum(jnp.where(perm[None, :] == request[:, None], ident[None, :], 0), axis=1)
    return slot_of * MAXLEN + positions - start_of


def row_stats(piece, weights, wanted):
    logits = jnp.dot(piece, weights, preferred_element_type=jnp.float32)
    top = jnp.max(logits, axis=1)
    expo = jnp.exp(logits - top[:, None])
    total = jnp.sum(expo, axis=1)
    moment = jnp.sum(expo * logits, axis=1)
    columns = jnp.arange(logits.shape[1], dtype=jnp.int32)
    picked = jnp.sum(jnp.where(columns[None, :] == wanted[:, None], logits, 0.0), axis=1)
    return jnp.stack([top, total, moment, picked], axis=0)


def on_device(hidden, gain, head, targets, lengths, perm):
    values = hidden.astype(jnp.float32)
    scale = lax.rsqrt(jnp.mean(values * values, axis=1, keepdims=True) + 1e-06)
    normed = (values * scale * gain.astype(jnp.float32)[None, :]).astype(jnp.bfloat16)
    n_tok = lax.axis_size("tok")
    n_voc = lax.axis_size("voc")
    local = normed.shape[0]
    group_rows = local * n_voc
    shard_cols = head.shape[1]
    col_base = lax.axis_index("voc") * shard_cols
    tok_index = lax.axis_index("tok")
    chunks = CHUNKS if local % (CHUNKS * 8) == 0 else 1
    step = local // chunks
    wanted = lax.dynamic_slice_in_dim(targets, tok_index * group_rows, group_rows, 0) - col_base
    wanted = wanted.reshape(n_voc, chunks, step)
    parts = []
    for j in range(chunks):
        piece = lax.all_gather(normed[j * step:(j + 1) * step], "voc", axis=0, tiled=True)
        parts.append(row_stats(piece, head, wanted[:, j, :].reshape(-1)).reshape(4, n_voc, step))
    stats = jnp.stack(parts, axis=2).reshape(4, group_rows)
    every = lax.all_gather(stats, "voc", axis=0)
    top = jnp.max(every[:, 0], axis=0)
    factor = jnp.exp(every[:, 0] - top[None, :])
    total = jnp.sum(every[:, 1] * factor, axis=0)
    moment = jnp.sum(every[:, 2] * factor, axis=0)
    picked = jnp.sum(every[:, 3], axis=0)
    lse = top + jnp.log(total)
    own = jnp.stack([picked - lse, lse - moment / total], axis=0)
    both = lax.all_gather(own, "tok", axis=1, tiled=True)
    out_rows = targets.shape[0] * 5 // 8 // (n_tok * n_voc)
    device = lax.axis_index(("tok", "voc"))
    positions = device * out_rows + jnp.arange(out_rows, dtype=jnp.int32)
    rows = slot_rows(positions, lengths, perm)
    return (both[0][rows], both[1][rows])


def solution(mesh):
    in_specs = (P(("tok", "voc"), None), P(), P(None, "voc"), P(), P(), P())
    out_specs = (P(("tok", "voc")), P(("tok", "voc")))
    return jax.shard_map(
        on_device, mesh=mesh, in_specs=in_specs, out_specs=out_specs, check_vma=False
    )
```

```python
import jax
import jax.numpy as jnp
from jax import lax
from jax.sharding import Mesh
from jax.sharding import PartitionSpec as P

MAXLEN = 1024
ALL = ("tok", "vz", "core")
VOC = ("vz", "core")


def slot_rows(positions, lengths, perm):
    count = lengths.shape[0]
    ident = jnp.arange(count, dtype=jnp.int32)
    starts = jnp.cumsum(lengths) - lengths
    request = jnp.sum((positions[:, None] >= starts[None, :]).astype(jnp.int32), axis=1) - 1
    start_of = jnp.sum(jnp.where(ident[None, :] == request[:, None], starts[None, :], 0), axis=1)
    slot_of = jnp.sum(jnp.where(perm[None, :] == request[:, None], ident[None, :], 0), axis=1)
    return slot_of * MAXLEN + positions - start_of


def row_stats(piece, weights, wanted):
    logits = jnp.dot(piece, weights, preferred_element_type=jnp.float32)
    top = jnp.max(logits, axis=1)
    expo = jnp.exp(logits - top[:, None])
    total = jnp.sum(expo, axis=1)
    moment = jnp.sum(expo * logits, axis=1)
    columns = jnp.arange(logits.shape[1], dtype=jnp.int32)
    picked = jnp.sum(jnp.where(columns[None, :] == wanted[:, None], logits, 0.0), axis=1)
    return jnp.stack([top, total, moment, picked], axis=0)


def on_device(hidden, gain, head, targets, lengths, perm):
    values = hidden.astype(jnp.float32)
    scale = lax.rsqrt(jnp.mean(values * values, axis=1, keepdims=True) + 1e-06)
    normed = (values * scale * gain.astype(jnp.float32)[None, :]).astype(jnp.bfloat16)
    n_tok = lax.axis_size("tok")
    nz = lax.axis_size("vz")
    n_core = lax.axis_size("core")
    n_voc = nz * n_core
    local = normed.shape[0]
    block = local * n_core
    group_rows = local * n_voc
    shard_cols = head.shape[1]
    u = lax.axis_index("vz")
    c = lax.axis_index("core")
    col_base = lax.axis_index(VOC) * shard_cols
    tok_index = lax.axis_index("tok")
    wanted = lax.dynamic_slice_in_dim(targets, tok_index * group_rows, group_rows, 0) - col_base
    stats = jnp.zeros((4, group_rows), jnp.float32)

    def place(stats, piece, start, size):
        got = row_stats(piece, head, lax.dynamic_slice_in_dim(wanted, start, size, 0))
        return lax.dynamic_update_slice_in_dim(stats, got, start, 1)

    def place_if(stats, valid, piece, start, size):
        start = jnp.clip(start, 0, group_rows - size)
        return lax.cond(valid, lambda s: place(s, piece, start, size), lambda s: s, stats)

    swap = [(i * n_core + k, i * n_core + (n_core - 1 - k)) for i in range(nz) for k in range(n_core)]
    peer = lax.ppermute(normed, VOC, swap)
    stats = place(stats, normed, (u * n_core + c) * local, local)
    stats = place(stats, peer, (u * n_core + 1 - c) * local, local)
    first = jnp.where(c == 0, jnp.concatenate([normed, peer], 0), jnp.concatenate([peer, normed], 0))
    line = [(i * n_core, (i + 1) * n_core) for i in range(nz - 1)]
    line += [(i * n_core + 1, (i - 1) * n_core + 1) for i in range(1, nz)]
    fwd = first
    for r in range(1, nz):
        recv = lax.ppermute(fwd, VOC, line)
        other = lax.ppermute(recv, VOC, swap)
        mine_from = jnp.where(c == 0, u - r, u + r)
        other_from = jnp.where(c == 0, u + r, u - r)
        stats = place_if(stats, (mine_from >= 0) & (mine_from < nz), recv, mine_from * block, block)
        stats = place_if(stats, (other_from >= 0) & (other_from < nz), other, other_from * block, block)
        fwd = recv
    every = lax.all_gather(stats, VOC, axis=0)
    top = jnp.max(every[:, 0], axis=0)
    factor = jnp.exp(every[:, 0] - top[None, :])
    total = jnp.sum(every[:, 1] * factor, axis=0)
    moment = jnp.sum(every[:, 2] * factor, axis=0)
    picked = jnp.sum(every[:, 3], axis=0)
    lse = top + jnp.log(total)
    own = jnp.stack([picked - lse, lse - moment / total], axis=0)
    both = lax.all_gather(own, "tok", axis=1, tiled=True)
    out_rows = targets.shape[0] * 5 // 8 // (n_tok * n_voc)
    device = lax.axis_index(ALL)
    positions = device * out_rows + jnp.arange(out_rows, dtype=jnp.int32)
    rows = slot_rows(positions, lengths, perm)
    return (both[0][rows], both[1][rows])


def solution(mesh):
    n_tok = mesh.shape["tok"]
    n_voc = mesh.shape["voc"]
    view = Mesh(mesh.devices.reshape(n_tok, n_voc // 2, 2), ALL)
    in_specs = (P(ALL, None), P(), P(None, VOC), P(), P(), P())
    out_specs = (P(ALL), P(ALL))
    return jax.shard_map(
        on_device, mesh=view, in_specs=in_specs, out_specs=out_specs, check_vma=False
    )
```

```python
import jax
import jax.numpy as jnp
from jax import lax
from jax.sharding import PartitionSpec as P
from jax.experimental import pallas as pl
from jax.experimental.pallas import tpu as pltpu

MAXLEN = 1024
CHUNKS = 2
TILE_N = 512
NEG = -1e30


def slot_rows(positions, lengths, perm):
    count = lengths.shape[0]
    ident = jnp.arange(count, dtype=jnp.int32)
    starts = jnp.cumsum(lengths) - lengths
    request = jnp.sum((positions[:, None] >= starts[None, :]).astype(jnp.int32), axis=1) - 1
    start_of = jnp.sum(jnp.where(ident[None, :] == request[:, None], starts[None, :], 0), axis=1)
    slot_of = jnp.sum(jnp.where(perm[None, :] == request[:, None], ident[None, :], 0), axis=1)
    return slot_of * MAXLEN + positions - start_of


def stats_kernel(ncols, x_ref, w_ref, t_ref, m_out, s_out, e_out, p_out, m_sc, s_sc, e_sc, p_sc):
    j = pl.program_id(1)
    tn = w_ref.shape[1]

    @pl.when(j == 0)
    def _():
        m_sc[...] = jnp.full(m_sc.shape, NEG, jnp.float32)
        s_sc[...] = jnp.zeros(s_sc.shape, jnp.float32)
        e_sc[...] = jnp.zeros(e_sc.shape, jnp.float32)
        p_sc[...] = jnp.zeros(p_sc.shape, jnp.float32)

    logits = jnp.dot(x_ref[...], w_ref[...], preferred_element_type=jnp.float32)
    cols = j * tn + lax.broadcasted_iota(jnp.int32, logits.shape, 1)
    logits = jnp.where(cols < ncols, logits, NEG)
    old = m_sc[...]
    new = jnp.maximum(old, jnp.max(logits, axis=1, keepdims=True))
    alpha = jnp.exp(old - new)
    expo = jnp.exp(logits - new)
    s_sc[...] = s_sc[...] * alpha + jnp.sum(expo, axis=1, keepdims=True)
    e_sc[...] = e_sc[...] * alpha + jnp.sum(expo * logits, axis=1, keepdims=True)
    p_sc[...] = p_sc[...] + jnp.sum(jnp.where(cols == t_ref[...], logits, 0.0), axis=1, keepdims=True)
    m_sc[...] = new

    @pl.when(j == pl.num_programs(1) - 1)
    def _():
        m_out[...] = m_sc[...]
        s_out[...] = s_sc[...]
        e_out[...] = e_sc[...]
        p_out[...] = p_sc[...]


def row_stats(piece, weights, wanted):
    rows, depth = piece.shape
    ncols = weights.shape[1]
    tm = min(512, rows)
    tn = TILE_N
    grid = (rows // tm, pl.cdiv(ncols, tn))
    wanted = jnp.where((wanted >= 0) & (wanted < ncols), wanted, -1).reshape(rows, 1)
    row_spec = pl.BlockSpec((tm, 1), lambda i, j: (i, 0))
    outs = pl.pallas_call(
        lambda *refs: stats_kernel(ncols, *refs),
        grid=grid,
        in_specs=[
            pl.BlockSpec((tm, depth), lambda i, j: (i, 0)),
            pl.BlockSpec((depth, tn), lambda i, j: (0, j)),
            row_spec,
        ],
        out_specs=[row_spec] * 4,
        out_shape=[jax.ShapeDtypeStruct((rows, 1), jnp.float32)] * 4,
        scratch_shapes=[pltpu.VMEM((tm, 1), jnp.float32)] * 4,
        compiler_params=pltpu.CompilerParams(
            dimension_semantics=("arbitrary", "arbitrary"), vmem_limit_bytes=48 * 1024 * 1024
        ),
        cost_estimate=pl.CostEstimate(
            flops=2 * rows * depth * ncols,
            transcendentals=rows * ncols,
            bytes_accessed=2 * depth * ncols * (rows // tm) + 2 * rows * depth,
        ),
    )(piece, weights, wanted)
    return jnp.stack([o.reshape(rows) for o in outs], axis=0)


def on_device(hidden, gain, head, targets, lengths, perm):
    values = hidden.astype(jnp.float32)
    scale = lax.rsqrt(jnp.mean(values * values, axis=1, keepdims=True) + 1e-06)
    normed = (values * scale * gain.astype(jnp.float32)[None, :]).astype(jnp.bfloat16)
    n_tok = lax.axis_size("tok")
    n_voc = lax.axis_size("voc")
    local = normed.shape[0]
    group_rows = local * n_voc
    shard_cols = head.shape[1]
    col_base = lax.axis_index("voc") * shard_cols
    tok_index = lax.axis_index("tok")
    chunks = CHUNKS if local % (CHUNKS * 8) == 0 else 1
    step = local // chunks
    wanted = lax.dynamic_slice_in_dim(targets, tok_index * group_rows, group_rows, 0) - col_base
    wanted = wanted.reshape(n_voc, chunks, step)
    parts = []
    for j in range(chunks):
        piece = lax.all_gather(normed[j * step:(j + 1) * step], "voc", axis=0, tiled=True)
        parts.append(row_stats(piece, head, wanted[:, j, :].reshape(-1)).reshape(4, n_voc, step))
    stats = jnp.stack(parts, axis=2).reshape(4, group_rows)
    every = lax.all_gather(stats, "voc", axis=0)
    top = jnp.max(every[:, 0], axis=0)
    factor = jnp.exp(every[:, 0] - top[None, :])
    total = jnp.sum(every[:, 1] * factor, axis=0)
    moment = jnp.sum(every[:, 2] * factor, axis=0)
    picked = jnp.sum(every[:, 3], axis=0)
    lse = top + jnp.log(total)
    own = jnp.stack([picked - lse, lse - moment / total], axis=0)
    both = lax.all_gather(own, "tok", axis=1, tiled=True)
    out_rows = targets.shape[0] * 5 // 8 // (n_tok * n_voc)
    device = lax.axis_index(("tok", "voc"))
    positions = device * out_rows + jnp.arange(out_rows, dtype=jnp.int32)
    rows = slot_rows(positions, lengths, perm)
    return (both[0][rows], both[1][rows])


def solution(mesh):
    in_specs = (P(("tok", "voc"), None), P(), P(None, "voc"), P(), P(), P())
    out_specs = (P(("tok", "voc")), P(("tok", "voc")))
    return jax.shard_map(
        on_device, mesh=mesh, in_specs=in_specs, out_specs=out_specs, check_vma=False
    )
```

```python
import jax
import jax.numpy as jnp
from jax import lax
from jax.sharding import PartitionSpec as P
from jax.experimental import pallas as pl
from jax.experimental.pallas import tpu as pltpu

MAXLEN = 1024
CHUNKS = 2
TILE_N = 512
NEG = -1e30


def slot_rows(positions, lengths, perm):
    count = lengths.shape[0]
    ident = jnp.arange(count, dtype=jnp.int32)
    starts = jnp.cumsum(lengths) - lengths
    request = jnp.sum((positions[:, None] >= starts[None, :]).astype(jnp.int32), axis=1) - 1
    start_of = jnp.sum(jnp.where(ident[None, :] == request[:, None], starts[None, :], 0), axis=1)
    slot_of = jnp.sum(jnp.where(perm[None, :] == request[:, None], ident[None, :], 0), axis=1)
    return slot_of * MAXLEN + positions - start_of


def stats_kernel(x_ref, w_ref, t_ref, m_out, s_out, e_out, p_out, m_sc, s_sc, e_sc, p_sc):
    j = pl.program_id(1)
    tn = w_ref.shape[0]

    @pl.when(j == 0)
    def _():
        m_sc[...] = jnp.full(m_sc.shape, NEG, jnp.float32)
        s_sc[...] = jnp.zeros(s_sc.shape, jnp.float32)
        e_sc[...] = jnp.zeros(e_sc.shape, jnp.float32)
        p_sc[...] = jnp.zeros(p_sc.shape, jnp.float32)

    logits = lax.dot_general(
        x_ref[...], w_ref[...], (((1,), (1,)), ((), ())), preferred_element_type=jnp.float32
    )
    old = m_sc[...]
    new = jnp.maximum(old, jnp.max(logits, axis=1, keepdims=True))
    alpha = jnp.exp(old - new)
    expo = jnp.exp(logits - new)
    s_sc[...] = s_sc[...] * alpha + jnp.sum(expo, axis=1, keepdims=True)
    e_sc[...] = e_sc[...] * alpha + jnp.sum(expo * logits, axis=1, keepdims=True)
    lanes = lax.broadcasted_iota(jnp.int32, logits.shape, 1)
    hit = lanes == t_ref[...] - j * tn
    p_sc[...] = p_sc[...] + jnp.sum(jnp.where(hit, logits, 0.0), axis=1, keepdims=True)
    m_sc[...] = new

    @pl.when(j == pl.num_programs(1) - 1)
    def _():
        m_out[...] = m_sc[...]
        s_out[...] = s_sc[...]
        e_out[...] = e_sc[...]
        p_out[...] = p_sc[...]


def dense_stats(piece, rows_t, wanted, base):
    logits = lax.dot_general(piece, rows_t, (((1,), (1,)), ((), ())), preferred_element_type=jnp.float32)
    top = jnp.max(logits, axis=1)
    expo = jnp.exp(logits - top[:, None])
    total = jnp.sum(expo, axis=1)
    moment = jnp.sum(expo * logits, axis=1)
    columns = base + jnp.arange(logits.shape[1], dtype=jnp.int32)
    picked = jnp.sum(jnp.where(columns[None, :] == wanted[:, None], logits, 0.0), axis=1)
    return top, total, moment, picked


def merge(a, b):
    top = jnp.maximum(a[0], b[0])
    fa, fb = jnp.exp(a[0] - top), jnp.exp(b[0] - top)
    return top, a[1] * fa + b[1] * fb, a[2] * fa + b[2] * fb, a[3] + b[3]


def row_stats(piece, weights_t, wanted):
    rows, depth = piece.shape
    ncols = weights_t.shape[0]
    tm = min(512, rows)
    tn = TILE_N
    full = ncols // tn
    wanted = jnp.where((wanted >= 0) & (wanted < ncols), wanted, -1)
    row_spec = pl.BlockSpec((tm, 1), lambda i, j: (i, 0))
    outs = pl.pallas_call(
        stats_kernel,
        grid=(rows // tm, full),
        in_specs=[
            pl.BlockSpec((tm, depth), lambda i, j: (i, 0)),
            pl.BlockSpec((tn, depth), lambda i, j: (j, 0)),
            row_spec,
        ],
        out_specs=[row_spec] * 4,
        out_shape=[jax.ShapeDtypeStruct((rows, 1), jnp.float32)] * 4,
        scratch_shapes=[pltpu.VMEM((tm, 1), jnp.float32)] * 4,
        compiler_params=pltpu.CompilerParams(
            dimension_semantics=("arbitrary", "arbitrary"), vmem_limit_bytes=48 * 1024 * 1024
        ),
        cost_estimate=pl.CostEstimate(
            flops=2 * rows * depth * full * tn,
            transcendentals=rows * full * tn,
            bytes_accessed=2 * depth * full * tn * (rows // tm) + 2 * rows * depth,
        ),
    )(piece, weights_t, wanted.reshape(rows, 1))
    got = tuple(o.reshape(rows) for o in outs)
    if full * tn < ncols:
        got = merge(got, dense_stats(piece, weights_t[full * tn:], wanted, full * tn))
    return jnp.stack(got, axis=0)


def on_device(hidden, gain, head, targets, lengths, perm):
    values = hidden.astype(jnp.float32)
    scale = lax.rsqrt(jnp.mean(values * values, axis=1, keepdims=True) + 1e-06)
    normed = (values * scale * gain.astype(jnp.float32)[None, :]).astype(jnp.bfloat16)
    n_tok = lax.axis_size("tok")
    n_voc = lax.axis_size("voc")
    local = normed.shape[0]
    group_rows = local * n_voc
    shard_cols = head.shape[1]
    col_base = lax.axis_index("voc") * shard_cols
    tok_index = lax.axis_index("tok")
    chunks = CHUNKS if local % (CHUNKS * 8) == 0 else 1
    step = local // chunks
    wanted = lax.dynamic_slice_in_dim(targets, tok_index * group_rows, group_rows, 0) - col_base
    wanted = wanted.reshape(n_voc, chunks, step)
    head_t = head.T
    parts = []
    for j in range(chunks):
        piece = lax.all_gather(normed[j * step:(j + 1) * step], "voc", axis=0, tiled=True)
        parts.append(row_stats(piece, head_t, wanted[:, j, :].reshape(-1)).reshape(4, n_voc, step))
    stats = jnp.stack(parts, axis=2).reshape(4, group_rows)
    every = lax.all_gather(stats, "voc", axis=0)
    top = jnp.max(every[:, 0], axis=0)
    factor = jnp.exp(every[:, 0] - top[None, :])
    total = jnp.sum(every[:, 1] * factor, axis=0)
    moment = jnp.sum(every[:, 2] * factor, axis=0)
    picked = jnp.sum(every[:, 3], axis=0)
    lse = top + jnp.log(total)
    own = jnp.stack([picked - lse, lse - moment / total], axis=0)
    both = lax.all_gather(own, "tok", axis=1, tiled=True)
    out_rows = targets.shape[0] * 5 // 8 // (n_tok * n_voc)
    device = lax.axis_index(("tok", "voc"))
    positions = device * out_rows + jnp.arange(out_rows, dtype=jnp.int32)
    rows = slot_rows(positions, lengths, perm)
    return (both[0][rows], both[1][rows])


def solution(mesh):
    in_specs = (P(("tok", "voc"), None), P(), P(None, "voc"), P(), P(), P())
    out_specs = (P(("tok", "voc")), P(("tok", "voc")))
    return jax.shard_map(
        on_device, mesh=mesh, in_specs=in_specs, out_specs=out_specs, check_vma=False
    )
```

```python
import jax
import jax.numpy as jnp
from jax import lax
from jax.sharding import PartitionSpec as P
from jax.experimental import pallas as pl
from jax.experimental.pallas import tpu as pltpu

MAXLEN = 1024
CHUNKS = 2
TILE_N = 512
NEG = -1e30


def slot_rows(positions, lengths, perm):
    count = lengths.shape[0]
    ident = jnp.arange(count, dtype=jnp.int32)
    starts = jnp.cumsum(lengths) - lengths
    request = jnp.sum((positions[:, None] >= starts[None, :]).astype(jnp.int32), axis=1) - 1
    start_of = jnp.sum(jnp.where(ident[None, :] == request[:, None], starts[None, :], 0), axis=1)
    slot_of = jnp.sum(jnp.where(perm[None, :] == request[:, None], ident[None, :], 0), axis=1)
    return slot_of * MAXLEN + positions - start_of


def stats_kernel(x_ref, w_ref, t_ref, m_out, s_out, e_out, p_out, m_sc, s_sc, e_sc, p_sc):
    j = pl.program_id(1)
    tn = w_ref.shape[0]
    lane = m_sc.shape[1]

    @pl.when(j == 0)
    def _():
        m_sc[...] = jnp.full(m_sc.shape, NEG, jnp.float32)
        s_sc[...] = jnp.zeros(s_sc.shape, jnp.float32)
        e_sc[...] = jnp.zeros(e_sc.shape, jnp.float32)
        p_sc[...] = jnp.zeros(p_sc.shape, jnp.float32)

    logits = lax.dot_general(
        x_ref[...], w_ref[...], (((1,), (1,)), ((), ())), preferred_element_type=jnp.float32
    )
    groups = [logits[:, k * lane:(k + 1) * lane] for k in range(tn // lane)]
    top = groups[0]
    for g in groups[1:]:
        top = jnp.maximum(top, g)
    old = m_sc[...]
    new = jnp.maximum(old, top)
    alpha = jnp.exp(old - new)
    total = s_sc[...] * alpha
    moment = e_sc[...] * alpha
    picked = p_sc[...]
    shift = t_ref[...] - j * tn
    lanes = lax.broadcasted_iota(jnp.int32, top.shape, 1)
    for k, g in enumerate(groups):
        expo = jnp.exp(g - new)
        total = total + expo
        moment = moment + expo * g
        picked = picked + jnp.where(lanes == shift - k * lane, g, 0.0)
    m_sc[...] = new
    s_sc[...] = total
    e_sc[...] = moment
    p_sc[...] = picked

    @pl.when(j == pl.num_programs(1) - 1)
    def _():
        m_out[...] = m_sc[...]
        s_out[...] = s_sc[...]
        e_out[...] = e_sc[...]
        p_out[...] = p_sc[...]


def dense_stats(piece, rows_t, wanted, base):
    logits = lax.dot_general(piece, rows_t, (((1,), (1,)), ((), ())), preferred_element_type=jnp.float32)
    top = jnp.max(logits, axis=1)
    expo = jnp.exp(logits - top[:, None])
    total = jnp.sum(expo, axis=1)
    moment = jnp.sum(expo * logits, axis=1)
    columns = base + jnp.arange(logits.shape[1], dtype=jnp.int32)
    picked = jnp.sum(jnp.where(columns[None, :] == wanted[:, None], logits, 0.0), axis=1)
    return top, total, moment, picked


def merge(a, b):
    top = jnp.maximum(a[0], b[0])
    fa, fb = jnp.exp(a[0] - top), jnp.exp(b[0] - top)
    return top, a[1] * fa + b[1] * fb, a[2] * fa + b[2] * fb, a[3] + b[3]


def row_stats(piece, weights_t, wanted):
    rows, depth = piece.shape
    ncols = weights_t.shape[0]
    tm = min(512, rows)
    tn = TILE_N
    lane = 128
    full = ncols // tn
    wanted = jnp.where((wanted >= 0) & (wanted < ncols), wanted, -1)
    got = None
    if full > 0:
        row_spec = pl.BlockSpec((tm, lane), lambda i, j: (i, 0))
        outs = pl.pallas_call(
            stats_kernel,
            grid=(rows // tm, full),
            in_specs=[
                pl.BlockSpec((tm, depth), lambda i, j: (i, 0)),
                pl.BlockSpec((tn, depth), lambda i, j: (j, 0)),
                row_spec,
            ],
            out_specs=[row_spec] * 4,
            out_shape=[jax.ShapeDtypeStruct((rows, lane), jnp.float32)] * 4,
            scratch_shapes=[pltpu.VMEM((tm, lane), jnp.float32)] * 4,
            compiler_params=pltpu.CompilerParams(
                dimension_semantics=("arbitrary", "arbitrary"), vmem_limit_bytes=48 * 1024 * 1024
            ),
            cost_estimate=pl.CostEstimate(
                flops=2 * rows * depth * full * tn,
                transcendentals=rows * full * tn,
                bytes_accessed=2 * depth * full * tn * (rows // tm) + 2 * rows * depth,
            ),
        )(piece, weights_t, jnp.broadcast_to(wanted[:, None], (rows, lane)))
        m, s, e, p = outs
        top = jnp.max(m, axis=1)
        scale = jnp.exp(m - top[:, None])
        got = (top, jnp.sum(s * scale, axis=1), jnp.sum(e * scale, axis=1), jnp.sum(p, axis=1))
    if full * tn < ncols:
        rest = dense_stats(piece, weights_t[full * tn:], wanted, full * tn)
        got = rest if got is None else merge(got, rest)
    return jnp.stack(got, axis=0)


def on_device(hidden, gain, head, targets, lengths, perm):
    values = hidden.astype(jnp.float32)
    scale = lax.rsqrt(jnp.mean(values * values, axis=1, keepdims=True) + 1e-06)
    normed = (values * scale * gain.astype(jnp.float32)[None, :]).astype(jnp.bfloat16)
    n_tok = lax.axis_size("tok")
    n_voc = lax.axis_size("voc")
    local = normed.shape[0]
    group_rows = local * n_voc
    shard_cols = head.shape[1]
    col_base = lax.axis_index("voc") * shard_cols
    tok_index = lax.axis_index("tok")
    chunks = CHUNKS if local % (CHUNKS * 8) == 0 else 1
    step = local // chunks
    wanted = lax.dynamic_slice_in_dim(targets, tok_index * group_rows, group_rows, 0) - col_base
    wanted = wanted.reshape(n_voc, chunks, step)
    head_t = head.T
    parts = []
    for j in range(chunks):
        piece = lax.all_gather(normed[j * step:(j + 1) * step], "voc", axis=0, tiled=True)
        parts.append(row_stats(piece, head_t, wanted[:, j, :].reshape(-1)).reshape(4, n_voc, step))
    stats = jnp.stack(parts, axis=2).reshape(4, group_rows)
    every = lax.all_gather(stats, "voc", axis=0)
    top = jnp.max(every[:, 0], axis=0)
    factor = jnp.exp(every[:, 0] - top[None, :])
    total = jnp.sum(every[:, 1] * factor, axis=0)
    moment = jnp.sum(every[:, 2] * factor, axis=0)
    picked = jnp.sum(every[:, 3], axis=0)
    lse = top + jnp.log(total)
    own = jnp.stack([picked - lse, lse - moment / total], axis=0)
    both = lax.all_gather(own, "tok", axis=1, tiled=True)
    out_rows = targets.shape[0] * 5 // 8 // (n_tok * n_voc)
    device = lax.axis_index(("tok", "voc"))
    positions = device * out_rows + jnp.arange(out_rows, dtype=jnp.int32)
    rows = slot_rows(positions, lengths, perm)
    return (both[0][rows], both[1][rows])


def solution(mesh):
    in_specs = (P(("tok", "voc"), None), P(), P(None, "voc"), P(), P(), P())
    out_specs = (P(("tok", "voc")), P(("tok", "voc")))
    return jax.shard_map(
        on_device, mesh=mesh, in_specs=in_specs, out_specs=out_specs, check_vma=False
    )
```

```python
import jax
import jax.numpy as jnp
from jax import lax
from jax.sharding import PartitionSpec as P
from jax.experimental import pallas as pl
from jax.experimental.pallas import tpu as pltpu

MAXLEN = 1024
CHUNKS = 2
TILE_N = 512
NEG = -1e30


def slot_rows(positions, lengths, perm):
    count = lengths.shape[0]
    ident = jnp.arange(count, dtype=jnp.int32)
    starts = jnp.cumsum(lengths) - lengths
    request = jnp.sum((positions[:, None] >= starts[None, :]).astype(jnp.int32), axis=1) - 1
    start_of = jnp.sum(jnp.where(ident[None, :] == request[:, None], starts[None, :], 0), axis=1)
    slot_of = jnp.sum(jnp.where(perm[None, :] == request[:, None], ident[None, :], 0), axis=1)
    return slot_of * MAXLEN + positions - start_of


def stats_kernel(ncols, x_ref, w_ref, t_ref, m_out, s_out, e_out, p_out, m_sc, s_sc, e_sc, p_sc):
    j = pl.program_id(1)
    last = pl.num_programs(1) - 1
    tn = w_ref.shape[0]
    lane = m_sc.shape[1]

    @pl.when(j == 0)
    def _():
        m_sc[...] = jnp.full(m_sc.shape, NEG, jnp.float32)
        s_sc[...] = jnp.zeros(s_sc.shape, jnp.float32)
        e_sc[...] = jnp.zeros(e_sc.shape, jnp.float32)
        p_sc[...] = jnp.zeros(p_sc.shape, jnp.float32)

    logits = lax.dot_general(
        x_ref[...], w_ref[...], (((1,), (1,)), ((), ())), preferred_element_type=jnp.float32
    )
    lanes = lax.broadcasted_iota(jnp.int32, m_sc.shape, 1)
    shift = t_ref[...] - j * tn

    def update(masked):
        groups = [logits[:, k * lane:(k + 1) * lane] for k in range(tn // lane)]
        if masked:
            groups = [jnp.where(lanes < ncols - j * tn - k * lane, g, NEG) for k, g in enumerate(groups)]
        top = groups[0]
        for g in groups[1:]:
            top = jnp.maximum(top, g)
        old = m_sc[...]
        new = jnp.maximum(old, top)
        alpha = jnp.exp(old - new)
        total = s_sc[...] * alpha
        moment = e_sc[...] * alpha
        picked = p_sc[...]
        for k, g in enumerate(groups):
            expo = jnp.exp(g - new)
            total = total + expo
            moment = moment + expo * g
            picked = picked + jnp.where(lanes == shift - k * lane, g, 0.0)
        m_sc[...] = new
        s_sc[...] = total
        e_sc[...] = moment
        p_sc[...] = picked

    if ncols % tn:
        pl.when(j < last)(lambda: update(False))
        pl.when(j == last)(lambda: update(True))
    else:
        update(False)

    @pl.when(j == last)
    def _():
        m = m_sc[...]
        top = jnp.max(m, axis=1, keepdims=True)
        scale = jnp.exp(m - top)
        m_out[...] = top
        s_out[...] = jnp.sum(s_sc[...] * scale, axis=1, keepdims=True)
        e_out[...] = jnp.sum(e_sc[...] * scale, axis=1, keepdims=True)
        p_out[...] = jnp.sum(p_sc[...], axis=1, keepdims=True)


def row_stats(piece, weights_t, wanted):
    rows, depth = piece.shape
    ncols = weights_t.shape[0]
    tm = min(512, rows)
    tn = TILE_N
    lane = 128
    steps = pl.cdiv(ncols, tn)
    wanted = jnp.where((wanted >= 0) & (wanted < ncols), wanted, -1)
    out_spec = pl.BlockSpec((tm, 1), lambda i, j: (i, 0))
    outs = pl.pallas_call(
        lambda *refs: stats_kernel(ncols, *refs),
        grid=(rows // tm, steps),
        in_specs=[
            pl.BlockSpec((tm, depth), lambda i, j: (i, 0)),
            pl.BlockSpec((tn, depth), lambda i, j: (j, 0)),
            pl.BlockSpec((tm, lane), lambda i, j: (i, 0)),
        ],
        out_specs=[out_spec] * 4,
        out_shape=[jax.ShapeDtypeStruct((rows, 1), jnp.float32)] * 4,
        scratch_shapes=[pltpu.VMEM((tm, lane), jnp.float32)] * 4,
        compiler_params=pltpu.CompilerParams(
            dimension_semantics=("arbitrary", "arbitrary"), vmem_limit_bytes=48 * 1024 * 1024
        ),
        cost_estimate=pl.CostEstimate(
            flops=2 * rows * depth * ncols,
            transcendentals=rows * ncols,
            bytes_accessed=2 * depth * ncols * (rows // tm) + 2 * rows * depth,
        ),
    )(piece, weights_t, jnp.broadcast_to(wanted[:, None], (rows, lane)))
    return jnp.stack([o.reshape(rows) for o in outs], axis=0)


def on_device(hidden, gain, head, targets, lengths, perm):
    values = hidden.astype(jnp.float32)
    scale = lax.rsqrt(jnp.mean(values * values, axis=1, keepdims=True) + 1e-06)
    normed = (values * scale * gain.astype(jnp.float32)[None, :]).astype(jnp.bfloat16)
    n_tok = lax.axis_size("tok")
    n_voc = lax.axis_size("voc")
    local = normed.shape[0]
    group_rows = local * n_voc
    shard_cols = head.shape[1]
    col_base = lax.axis_index("voc") * shard_cols
    tok_index = lax.axis_index("tok")
    chunks = CHUNKS if local % (CHUNKS * 8) == 0 else 1
    step = local // chunks
    wanted = lax.dynamic_slice_in_dim(targets, tok_index * group_rows, group_rows, 0) - col_base
    wanted = wanted.reshape(n_voc, chunks, step)
    head_t = head.T
    parts = []
    for j in range(chunks):
        piece = lax.all_gather(normed[j * step:(j + 1) * step], "voc", axis=0, tiled=True)
        parts.append(row_stats(piece, head_t, wanted[:, j, :].reshape(-1)).reshape(4, n_voc, step))
    stats = jnp.stack(parts, axis=2).reshape(4, group_rows)
    every = lax.all_gather(stats, "voc", axis=0)
    top = jnp.max(every[:, 0], axis=0)
    factor = jnp.exp(every[:, 0] - top[None, :])
    total = jnp.sum(every[:, 1] * factor, axis=0)
    moment = jnp.sum(every[:, 2] * factor, axis=0)
    picked = jnp.sum(every[:, 3], axis=0)
    lse = top + jnp.log(total)
    own = jnp.stack([picked - lse, lse - moment / total], axis=0)
    both = lax.all_gather(own, "tok", axis=1, tiled=True)
    out_rows = targets.shape[0] * 5 // 8 // (n_tok * n_voc)
    device = lax.axis_index(("tok", "voc"))
    positions = device * out_rows + jnp.arange(out_rows, dtype=jnp.int32)
    rows = slot_rows(positions, lengths, perm)
    return (both[0][rows], both[1][rows])


def solution(mesh):
    in_specs = (P(("tok", "voc"), None), P(), P(None, "voc"), P(), P(), P())
    out_specs = (P(("tok", "voc")), P(("tok", "voc")))
    return jax.shard_map(
        on_device, mesh=mesh, in_specs=in_specs, out_specs=out_specs, check_vma=False
    )
```

```python
import jax
import jax.numpy as jnp
from jax import lax
from jax.sharding import PartitionSpec as P
from jax.experimental import pallas as pl
from jax.experimental.pallas import tpu as pltpu

MAXLEN = 1024
CHUNKS = 4
TILE_N = 512
NEG = -1e30


def slot_rows(positions, lengths, perm):
    count = lengths.shape[0]
    ident = jnp.arange(count, dtype=jnp.int32)
    starts = jnp.cumsum(lengths) - lengths
    request = jnp.sum((positions[:, None] >= starts[None, :]).astype(jnp.int32), axis=1) - 1
    start_of = jnp.sum(jnp.where(ident[None, :] == request[:, None], starts[None, :], 0), axis=1)
    slot_of = jnp.sum(jnp.where(perm[None, :] == request[:, None], ident[None, :], 0), axis=1)
    return slot_of * MAXLEN + positions - start_of


def stats_kernel(ncols, x_ref, w_ref, t_ref, m_out, s_out, e_out, p_out, m_sc, s_sc, e_sc, p_sc):
    j = pl.program_id(1)
    last = pl.num_programs(1) - 1
    tn = w_ref.shape[0]
    lane = m_sc.shape[1]

    @pl.when(j == 0)
    def _():
        m_sc[...] = jnp.full(m_sc.shape, NEG, jnp.float32)
        s_sc[...] = jnp.zeros(s_sc.shape, jnp.float32)
        e_sc[...] = jnp.zeros(e_sc.shape, jnp.float32)
        p_sc[...] = jnp.zeros(p_sc.shape, jnp.float32)

    logits = lax.dot_general(
        x_ref[...], w_ref[...], (((1,), (1,)), ((), ())), preferred_element_type=jnp.float32
    )
    lanes = lax.broadcasted_iota(jnp.int32, m_sc.shape, 1)
    shift = t_ref[...] - j * tn

    def update(masked):
        groups = [logits[:, k * lane:(k + 1) * lane] for k in range(tn // lane)]
        if masked:
            groups = [jnp.where(lanes < ncols - j * tn - k * lane, g, NEG) for k, g in enumerate(groups)]
        top = groups[0]
        for g in groups[1:]:
            top = jnp.maximum(top, g)
        old = m_sc[...]
        new = jnp.maximum(old, top)
        alpha = jnp.exp(old - new)
        total = s_sc[...] * alpha
        moment = e_sc[...] * alpha
        picked = p_sc[...]
        for k, g in enumerate(groups):
            expo = jnp.exp(g - new)
            total = total + expo
            moment = moment + expo * g
            picked = picked + jnp.where(lanes == shift - k * lane, g, 0.0)
        m_sc[...] = new
        s_sc[...] = total
        e_sc[...] = moment
        p_sc[...] = picked

    if ncols % tn:
        pl.when(j < last)(lambda: update(False))
        pl.when(j == last)(lambda: update(True))
    else:
        update(False)

    @pl.when(j == last)
    def _():
        m = m_sc[...]
        top = jnp.max(m, axis=1, keepdims=True)
        scale = jnp.exp(m - top)
        m_out[...] = top
        s_out[...] = jnp.sum(s_sc[...] * scale, axis=1, keepdims=True)
        e_out[...] = jnp.sum(e_sc[...] * scale, axis=1, keepdims=True)
        p_out[...] = jnp.sum(p_sc[...], axis=1, keepdims=True)


def row_stats(piece, weights_t, wanted):
    rows, depth = piece.shape
    ncols = weights_t.shape[0]
    tm = min(512, rows)
    tn = TILE_N
    lane = 128
    steps = pl.cdiv(ncols, tn)
    wanted = jnp.where((wanted >= 0) & (wanted < ncols), wanted, -1)
    out_spec = pl.BlockSpec((tm, 1), lambda i, j: (i, 0))
    outs = pl.pallas_call(
        lambda *refs: stats_kernel(ncols, *refs),
        grid=(rows // tm, steps),
        in_specs=[
            pl.BlockSpec((tm, depth), lambda i, j: (i, 0)),
            pl.BlockSpec((tn, depth), lambda i, j: (j, 0)),
            pl.BlockSpec((tm, lane), lambda i, j: (i, 0)),
        ],
        out_specs=[out_spec] * 4,
        out_shape=[jax.ShapeDtypeStruct((rows, 1), jnp.float32)] * 4,
        scratch_shapes=[pltpu.VMEM((tm, lane), jnp.float32)] * 4,
        compiler_params=pltpu.CompilerParams(
            dimension_semantics=("arbitrary", "arbitrary"), vmem_limit_bytes=48 * 1024 * 1024
        ),
        cost_estimate=pl.CostEstimate(
            flops=2 * rows * depth * ncols,
            transcendentals=rows * ncols,
            bytes_accessed=2 * depth * ncols * (rows // tm) + 2 * rows * depth,
        ),
    )(piece, weights_t, jnp.broadcast_to(wanted[:, None], (rows, lane)))
    return jnp.stack([o.reshape(rows) for o in outs], axis=0)


def on_device(hidden, gain, head, targets, lengths, perm):
    values = hidden.astype(jnp.float32)
    scale = lax.rsqrt(jnp.mean(values * values, axis=1, keepdims=True) + 1e-06)
    normed = (values * scale * gain.astype(jnp.float32)[None, :]).astype(jnp.bfloat16)
    n_tok = lax.axis_size("tok")
    n_voc = lax.axis_size("voc")
    local = normed.shape[0]
    group_rows = local * n_voc
    shard_cols = head.shape[1]
    col_base = lax.axis_index("voc") * shard_cols
    tok_index = lax.axis_index("tok")
    chunks = CHUNKS if local % (CHUNKS * 8) == 0 else 1
    step = local // chunks
    wanted = lax.dynamic_slice_in_dim(targets, tok_index * group_rows, group_rows, 0) - col_base
    wanted = wanted.reshape(n_voc, chunks, step)
    head_t = head.T
    parts = []
    for j in range(chunks):
        piece = lax.all_gather(normed[j * step:(j + 1) * step], "voc", axis=0, tiled=True)
        stats = row_stats(piece, head_t, wanted[:, j, :].reshape(-1))
        every = lax.all_gather(stats, "voc", axis=0)
        top = jnp.max(every[:, 0], axis=0)
        factor = jnp.exp(every[:, 0] - top[None, :])
        total = jnp.sum(every[:, 1] * factor, axis=0)
        moment = jnp.sum(every[:, 2] * factor, axis=0)
        picked = jnp.sum(every[:, 3], axis=0)
        lse = top + jnp.log(total)
        parts.append(jnp.stack([picked - lse, lse - moment / total], axis=0).reshape(2, n_voc, step))
    own = jnp.stack(parts, axis=2).reshape(2, group_rows)
    both = lax.all_gather(own, "tok", axis=1, tiled=True)
    out_rows = targets.shape[0] * 5 // 8 // (n_tok * n_voc)
    device = lax.axis_index(("tok", "voc"))
    positions = device * out_rows + jnp.arange(out_rows, dtype=jnp.int32)
    rows = slot_rows(positions, lengths, perm)
    picked_out = jnp.take(both, rows, axis=1)
    return (picked_out[0], picked_out[1])


def solution(mesh):
    in_specs = (P(("tok", "voc"), None), P(), P(None, "voc"), P(), P(), P())
    out_specs = (P(("tok", "voc")), P(("tok", "voc")))
    return jax.shard_map(
        on_device, mesh=mesh, in_specs=in_specs, out_specs=out_specs, check_vma=False
    )
```

```python
import jax
import jax.numpy as jnp
from jax import lax
from jax.sharding import PartitionSpec as P
from jax.experimental import pallas as pl
from jax.experimental.pallas import tpu as pltpu

MAXLEN = 1024
CHUNKS = 2
TILE_N = 512
NEG = -1e30


def slot_rows(positions, lengths, perm):
    count = lengths.shape[0]
    ident = jnp.arange(count, dtype=jnp.int32)
    starts = jnp.cumsum(lengths) - lengths
    request = jnp.sum((positions[:, None] >= starts[None, :]).astype(jnp.int32), axis=1) - 1
    start_of = jnp.sum(jnp.where(ident[None, :] == request[:, None], starts[None, :], 0), axis=1)
    slot_of = jnp.sum(jnp.where(perm[None, :] == request[:, None], ident[None, :], 0), axis=1)
    return slot_of * MAXLEN + positions - start_of


def stats_kernel(ncols, x_ref, w_ref, t_ref, m_out, s_out, e_out, p_out, m_sc, s_sc, e_sc, p_sc):
    j = pl.program_id(1)
    last = pl.num_programs(1) - 1
    tn = w_ref.shape[0]
    lane = m_sc.shape[1]

    @pl.when(j == 0)
    def _():
        m_sc[...] = jnp.full(m_sc.shape, NEG, jnp.float32)
        s_sc[...] = jnp.zeros(s_sc.shape, jnp.float32)
        e_sc[...] = jnp.zeros(e_sc.shape, jnp.float32)
        p_sc[...] = jnp.zeros(p_sc.shape, jnp.float32)

    logits = lax.dot_general(
        x_ref[...], w_ref[...], (((1,), (1,)), ((), ())), preferred_element_type=jnp.float32
    )
    lanes = lax.broadcasted_iota(jnp.int32, m_sc.shape, 1)
    shift = t_ref[...] - j * tn

    def update(masked):
        groups = [logits[:, k * lane:(k + 1) * lane] for k in range(tn // lane)]
        if masked:
            groups = [jnp.where(lanes < ncols - j * tn - k * lane, g, NEG) for k, g in enumerate(groups)]
        top = groups[0]
        for g in groups[1:]:
            top = jnp.maximum(top, g)
        old = m_sc[...]
        new = jnp.maximum(old, top)
        alpha = jnp.exp(old - new)
        total = s_sc[...] * alpha
        moment = e_sc[...] * alpha
        picked = p_sc[...]
        for k, g in enumerate(groups):
            expo = jnp.exp(g - new)
            total = total + expo
            moment = moment + expo * g
            picked = picked + jnp.where(lanes == shift - k * lane, g, 0.0)
        m_sc[...] = new
        s_sc[...] = total
        e_sc[...] = moment
        p_sc[...] = picked

    if ncols % tn:
        pl.when(j < last)(lambda: update(False))
        pl.when(j == last)(lambda: update(True))
    else:
        update(False)

    @pl.when(j == last)
    def _():
        m = m_sc[...]
        top = jnp.max(m, axis=1, keepdims=True)
        scale = jnp.exp(m - top)
        m_out[...] = top
        s_out[...] = jnp.sum(s_sc[...] * scale, axis=1, keepdims=True)
        e_out[...] = jnp.sum(e_sc[...] * scale, axis=1, keepdims=True)
        p_out[...] = jnp.sum(p_sc[...], axis=1, keepdims=True)


def row_stats(piece, weights_t, wanted):
    rows, depth = piece.shape
    ncols = weights_t.shape[0]
    tm = min(512, rows)
    tn = TILE_N
    lane = 128
    steps = pl.cdiv(ncols, tn)
    wanted = jnp.where((wanted >= 0) & (wanted < ncols), wanted, -1)
    out_spec = pl.BlockSpec((tm, 1), lambda i, j: (i, 0))
    outs = pl.pallas_call(
        lambda *refs: stats_kernel(ncols, *refs),
        grid=(rows // tm, steps),
        in_specs=[
            pl.BlockSpec((tm, depth), lambda i, j: (i, 0)),
            pl.BlockSpec((tn, depth), lambda i, j: (j, 0)),
            pl.BlockSpec((tm, lane), lambda i, j: (i, 0)),
        ],
        out_specs=[out_spec] * 4,
        out_shape=[jax.ShapeDtypeStruct((rows, 1), jnp.float32)] * 4,
        scratch_shapes=[pltpu.VMEM((tm, lane), jnp.float32)] * 4,
        compiler_params=pltpu.CompilerParams(
            dimension_semantics=("arbitrary", "arbitrary"), vmem_limit_bytes=48 * 1024 * 1024
        ),
        cost_estimate=pl.CostEstimate(
            flops=2 * rows * depth * ncols,
            transcendentals=rows * ncols,
            bytes_accessed=2 * depth * ncols * (rows // tm) + 2 * rows * depth,
        ),
    )(piece, weights_t, jnp.broadcast_to(wanted[:, None], (rows, lane)))
    return jnp.stack([o.reshape(rows) for o in outs], axis=0)


def on_device(hidden, gain, head, targets, lengths, perm):
    def norm(part):
        values = part.astype(jnp.float32)
        scale = lax.rsqrt(jnp.mean(values * values, axis=1, keepdims=True) + 1e-06)
        return (values * scale * gain.astype(jnp.float32)[None, :]).astype(jnp.bfloat16)

    n_tok = lax.axis_size("tok")
    n_voc = lax.axis_size("voc")
    local = hidden.shape[0]
    group_rows = local * n_voc
    shard_cols = head.shape[1]
    col_base = lax.axis_index("voc") * shard_cols
    tok_index = lax.axis_index("tok")
    chunks = CHUNKS if local % (CHUNKS * 8) == 0 else 1
    step = local // chunks
    wanted = lax.dynamic_slice_in_dim(targets, tok_index * group_rows, group_rows, 0) - col_base
    wanted = wanted.reshape(n_voc, chunks, step)
    head_t = head.T
    parts = []
    for j in range(chunks):
        piece = lax.all_gather(norm(hidden[j * step:(j + 1) * step]), "voc", axis=0, tiled=True)
        parts.append(row_stats(piece, head_t, wanted[:, j, :].reshape(-1)).reshape(4, n_voc, step))
    stats = jnp.stack(parts, axis=2).reshape(4, group_rows)
    every = lax.all_gather(stats, "voc", axis=0)
    top = jnp.max(every[:, 0], axis=0)
    factor = jnp.exp(every[:, 0] - top[None, :])
    total = jnp.sum(every[:, 1] * factor, axis=0)
    moment = jnp.sum(every[:, 2] * factor, axis=0)
    picked = jnp.sum(every[:, 3], axis=0)
    lse = top + jnp.log(total)
    own = jnp.stack([picked - lse, lse - moment / total], axis=0)
    both = lax.all_gather(own, "tok", axis=1, tiled=True)
    out_rows = targets.shape[0] * 5 // 8 // (n_tok * n_voc)
    device = lax.axis_index(("tok", "voc"))
    positions = device * out_rows + jnp.arange(out_rows, dtype=jnp.int32)
    rows = slot_rows(positions, lengths, perm)
    picked_out = jnp.take(both, rows, axis=1)
    return (picked_out[0], picked_out[1])


def solution(mesh):
    in_specs = (P(("tok", "voc"), None), P(), P(None, "voc"), P(), P(), P())
    out_specs = (P(("tok", "voc")), P(("tok", "voc")))
    return jax.shard_map(
        on_device, mesh=mesh, in_specs=in_specs, out_specs=out_specs, check_vma=False
    )
```

```python
import jax
import jax.numpy as jnp
from jax import lax
from jax.sharding import PartitionSpec as P
from jax.experimental import pallas as pl
from jax.experimental.pallas import tpu as pltpu

MAXLEN = 1024
CHUNKS = 2
TILE_N = 512
NEG = -1e30


def slot_rows(positions, lengths, perm):
    count = lengths.shape[0]
    ident = jnp.arange(count, dtype=jnp.int32)
    starts = jnp.cumsum(lengths) - lengths
    request = jnp.sum((positions[:, None] >= starts[None, :]).astype(jnp.int32), axis=1) - 1
    start_of = jnp.sum(jnp.where(ident[None, :] == request[:, None], starts[None, :], 0), axis=1)
    slot_of = jnp.sum(jnp.where(perm[None, :] == request[:, None], ident[None, :], 0), axis=1)
    return slot_of * MAXLEN + positions - start_of


def stats_kernel(ncols, x_ref, w_ref, t_ref, m_out, s_out, e_out, p_out, m_sc, s_sc, e_sc, p_sc):
    j = pl.program_id(1)
    last = pl.num_programs(1) - 1
    tn = w_ref.shape[0]
    lane = m_sc.shape[1]

    @pl.when(j == 0)
    def _():
        m_sc[...] = jnp.full(m_sc.shape, NEG, jnp.float32)
        s_sc[...] = jnp.zeros(s_sc.shape, jnp.float32)
        e_sc[...] = jnp.zeros(e_sc.shape, jnp.float32)
        p_sc[...] = jnp.zeros(p_sc.shape, jnp.float32)

    halves = 2
    width = tn // halves
    x = x_ref[...]
    lanes = lax.broadcasted_iota(jnp.int32, m_sc.shape, 1)
    shift = t_ref[...] - j * tn

    def update(masked):
        total = s_sc[...]
        moment = e_sc[...]
        picked = p_sc[...]
        old = m_sc[...]
        for h in range(halves):
            part = lax.dot_general(
                x, w_ref[h * width:(h + 1) * width, :], (((1,), (1,)), ((), ())),
                preferred_element_type=jnp.float32,
            )
            base = h * width
            groups = [part[:, k * lane:(k + 1) * lane] for k in range(width // lane)]
            if masked:
                groups = [
                    jnp.where(lanes < ncols - j * tn - base - k * lane, g, NEG) for k, g in enumerate(groups)
                ]
            top = groups[0]
            for g in groups[1:]:
                top = jnp.maximum(top, g)
            new = jnp.maximum(old, top)
            alpha = jnp.exp(old - new)
            total = total * alpha
            moment = moment * alpha
            for k, g in enumerate(groups):
                expo = jnp.exp(g - new)
                total = total + expo
                moment = moment + expo * g
                picked = picked + jnp.where(lanes == shift - base - k * lane, g, 0.0)
            old = new
        m_sc[...] = old
        s_sc[...] = total
        e_sc[...] = moment
        p_sc[...] = picked

    if ncols % tn:
        pl.when(j < last)(lambda: update(False))
        pl.when(j == last)(lambda: update(True))
    else:
        update(False)

    @pl.when(j == last)
    def _():
        m = m_sc[...]
        top = jnp.max(m, axis=1, keepdims=True)
        scale = jnp.exp(m - top)
        m_out[...] = top
        s_out[...] = jnp.sum(s_sc[...] * scale, axis=1, keepdims=True)
        e_out[...] = jnp.sum(e_sc[...] * scale, axis=1, keepdims=True)
        p_out[...] = jnp.sum(p_sc[...], axis=1, keepdims=True)


def row_stats(piece, weights_t, wanted):
    rows, depth = piece.shape
    ncols = weights_t.shape[0]
    tm = min(512, rows)
    tn = TILE_N
    lane = 128
    steps = pl.cdiv(ncols, tn)
    wanted = jnp.where((wanted >= 0) & (wanted < ncols), wanted, -1)
    out_spec = pl.BlockSpec((tm, 1), lambda i, j: (i, 0))
    outs = pl.pallas_call(
        lambda *refs: stats_kernel(ncols, *refs),
        grid=(rows // tm, steps),
        in_specs=[
            pl.BlockSpec((tm, depth), lambda i, j: (i, 0)),
            pl.BlockSpec((tn, depth), lambda i, j: (j, 0)),
            pl.BlockSpec((tm, lane), lambda i, j: (i, 0)),
        ],
        out_specs=[out_spec] * 4,
        out_shape=[jax.ShapeDtypeStruct((rows, 1), jnp.float32)] * 4,
        scratch_shapes=[pltpu.VMEM((tm, lane), jnp.float32)] * 4,
        compiler_params=pltpu.CompilerParams(
            dimension_semantics=("arbitrary", "arbitrary"), vmem_limit_bytes=48 * 1024 * 1024
        ),
        cost_estimate=pl.CostEstimate(
            flops=2 * rows * depth * ncols,
            transcendentals=rows * ncols,
            bytes_accessed=2 * depth * ncols * (rows // tm) + 2 * rows * depth,
        ),
    )(piece, weights_t, jnp.broadcast_to(wanted[:, None], (rows, lane)))
    return jnp.stack([o.reshape(rows) for o in outs], axis=0)


def on_device(hidden, gain, head, targets, lengths, perm):
    values = hidden.astype(jnp.float32)
    scale = lax.rsqrt(jnp.mean(values * values, axis=1, keepdims=True) + 1e-06)
    normed = (values * scale * gain.astype(jnp.float32)[None, :]).astype(jnp.bfloat16)
    n_tok = lax.axis_size("tok")
    n_voc = lax.axis_size("voc")
    local = normed.shape[0]
    group_rows = local * n_voc
    shard_cols = head.shape[1]
    col_base = lax.axis_index("voc") * shard_cols
    tok_index = lax.axis_index("tok")
    chunks = CHUNKS if local % (CHUNKS * 8) == 0 else 1
    step = local // chunks
    wanted = lax.dynamic_slice_in_dim(targets, tok_index * group_rows, group_rows, 0) - col_base
    wanted = wanted.reshape(n_voc, chunks, step)
    head_t = head.T
    parts = []
    for j in range(chunks):
        piece = lax.all_gather(normed[j * step:(j + 1) * step], "voc", axis=0, tiled=True)
        parts.append(row_stats(piece, head_t, wanted[:, j, :].reshape(-1)).reshape(4, n_voc, step))
    stats = jnp.stack(parts, axis=2).reshape(4, group_rows)
    every = lax.all_gather(stats, "voc", axis=0)
    top = jnp.max(every[:, 0], axis=0)
    factor = jnp.exp(every[:, 0] - top[None, :])
    total = jnp.sum(every[:, 1] * factor, axis=0)
    moment = jnp.sum(every[:, 2] * factor, axis=0)
    picked = jnp.sum(every[:, 3], axis=0)
    lse = top + jnp.log(total)
    own = jnp.stack([picked - lse, lse - moment / total], axis=0)
    both = lax.all_gather(own, "tok", axis=1, tiled=True)
    out_rows = targets.shape[0] * 5 // 8 // (n_tok * n_voc)
    device = lax.axis_index(("tok", "voc"))
    positions = device * out_rows + jnp.arange(out_rows, dtype=jnp.int32)
    rows = slot_rows(positions, lengths, perm)
    return (both[0][rows], both[1][rows])


def solution(mesh):
    in_specs = (P(("tok", "voc"), None), P(), P(None, "voc"), P(), P(), P())
    out_specs = (P(("tok", "voc")), P(("tok", "voc")))
    return jax.shard_map(
        on_device, mesh=mesh, in_specs=in_specs, out_specs=out_specs, check_vma=False
    )
```

```python
import jax
import jax.numpy as jnp
from jax import lax
from jax.sharding import PartitionSpec as P
from jax.experimental import pallas as pl
from jax.experimental.pallas import tpu as pltpu

MAXLEN = 1024
TILE_N = 512
NEG = -1e30


def slot_rows(positions, lengths, perm):
    count = lengths.shape[0]
    ident = jnp.arange(count, dtype=jnp.int32)
    starts = jnp.cumsum(lengths) - lengths
    request = jnp.sum((positions[:, None] >= starts[None, :]).astype(jnp.int32), axis=1) - 1
    start_of = jnp.sum(jnp.where(ident[None, :] == request[:, None], starts[None, :], 0), axis=1)
    slot_of = jnp.sum(jnp.where(perm[None, :] == request[:, None], ident[None, :], 0), axis=1)
    return slot_of * MAXLEN + positions - start_of


def stats_kernel(ncols, x_ref, w_ref, t_ref, m_out, s_out, e_out, p_out, m_sc, s_sc, e_sc, p_sc):
    j = pl.program_id(1)
    last = pl.num_programs(1) - 1
    tn = w_ref.shape[0]
    lane = m_sc.shape[1]

    @pl.when(j == 0)
    def _():
        m_sc[...] = jnp.full(m_sc.shape, NEG, jnp.float32)
        s_sc[...] = jnp.zeros(s_sc.shape, jnp.float32)
        e_sc[...] = jnp.zeros(e_sc.shape, jnp.float32)
        p_sc[...] = jnp.zeros(p_sc.shape, jnp.float32)

    logits = lax.dot_general(
        x_ref[...], w_ref[...], (((1,), (1,)), ((), ())), preferred_element_type=jnp.float32
    )
    lanes = lax.broadcasted_iota(jnp.int32, m_sc.shape, 1)
    shift = t_ref[...] - j * tn

    def update(masked):
        groups = [logits[:, k * lane:(k + 1) * lane] for k in range(tn // lane)]
        if masked:
            groups = [jnp.where(lanes < ncols - j * tn - k * lane, g, NEG) for k, g in enumerate(groups)]
        top = groups[0]
        for g in groups[1:]:
            top = jnp.maximum(top, g)
        old = m_sc[...]
        new = jnp.maximum(old, top)
        alpha = jnp.exp(old - new)
        total = s_sc[...] * alpha
        moment = e_sc[...] * alpha
        picked = p_sc[...]
        for k, g in enumerate(groups):
            expo = jnp.exp(g - new)
            total = total + expo
            moment = moment + expo * g
            picked = picked + jnp.where(lanes == shift - k * lane, g, 0.0)
        m_sc[...] = new
        s_sc[...] = total
        e_sc[...] = moment
        p_sc[...] = picked

    if ncols % tn:
        pl.when(j < last)(lambda: update(False))
        pl.when(j == last)(lambda: update(True))
    else:
        update(False)

    @pl.when(j == last)
    def _():
        m = m_sc[...]
        top = jnp.max(m, axis=1, keepdims=True)
        scale = jnp.exp(m - top)
        m_out[...] = top
        s_out[...] = jnp.sum(s_sc[...] * scale, axis=1, keepdims=True)
        e_out[...] = jnp.sum(e_sc[...] * scale, axis=1, keepdims=True)
        p_out[...] = jnp.sum(p_sc[...], axis=1, keepdims=True)


def row_stats(piece, weights_t, wanted):
    rows, depth = piece.shape
    ncols = weights_t.shape[0]
    tm = rows if rows <= 512 else (rows // 2 if rows % 16 == 0 and rows <= 1024 else 512)
    tn = TILE_N
    lane = 128
    steps = pl.cdiv(ncols, tn)
    wanted = jnp.where((wanted >= 0) & (wanted < ncols), wanted, -1)
    out_spec = pl.BlockSpec((tm, 1), lambda i, j: (i, 0))
    outs = pl.pallas_call(
        lambda *refs: stats_kernel(ncols, *refs),
        grid=(rows // tm, steps),
        in_specs=[
            pl.BlockSpec((tm, depth), lambda i, j: (i, 0)),
            pl.BlockSpec((tn, depth), lambda i, j: (j, 0)),
            pl.BlockSpec((tm, lane), lambda i, j: (i, 0)),
        ],
        out_specs=[out_spec] * 4,
        out_shape=[jax.ShapeDtypeStruct((rows, 1), jnp.float32)] * 4,
        scratch_shapes=[pltpu.VMEM((tm, lane), jnp.float32)] * 4,
        compiler_params=pltpu.CompilerParams(
            dimension_semantics=("arbitrary", "arbitrary"), vmem_limit_bytes=48 * 1024 * 1024
        ),
        cost_estimate=pl.CostEstimate(
            flops=2 * rows * depth * ncols,
            transcendentals=rows * ncols,
            bytes_accessed=2 * depth * ncols * (rows // tm) + 2 * rows * depth,
        ),
    )(piece, weights_t, jnp.broadcast_to(wanted[:, None], (rows, lane)))
    return jnp.stack([o.reshape(rows) for o in outs], axis=0)


def on_device(hidden, gain, head, targets, lengths, perm):
    def norm(part):
        values = part.astype(jnp.float32)
        scale = lax.rsqrt(jnp.mean(values * values, axis=1, keepdims=True) + 1e-06)
        return (values * scale * gain.astype(jnp.float32)[None, :]).astype(jnp.bfloat16)

    n_tok = lax.axis_size("tok")
    n_voc = lax.axis_size("voc")
    local = hidden.shape[0]
    group_rows = local * n_voc
    shard_cols = head.shape[1]
    col_base = lax.axis_index("voc") * shard_cols
    tok_index = lax.axis_index("tok")
    unit = local // 8
    bounds = [0, 2 * unit, 5 * unit, local] if local % 64 == 0 else [0, local]
    wanted = lax.dynamic_slice_in_dim(targets, tok_index * group_rows, group_rows, 0) - col_base
    wanted = wanted.reshape(n_voc, local)
    head_t = head.T
    parts = []
    rest = hidden
    for lo, hi in zip(bounds[:-1], bounds[1:]):
        normed = norm(rest[lo:hi])
        normed, rest = lax.optimization_barrier((normed, rest))
        piece = lax.all_gather(normed, "voc", axis=0, tiled=True)
        got = row_stats(piece, head_t, wanted[:, lo:hi].reshape(-1))
        parts.append(got.reshape(4, n_voc, hi - lo))
    stats = jnp.concatenate(parts, axis=2).reshape(4, group_rows)
    every = lax.all_gather(stats, "voc", axis=0)
    top = jnp.max(every[:, 0], axis=0)
    factor = jnp.exp(every[:, 0] - top[None, :])
    total = jnp.sum(every[:, 1] * factor, axis=0)
    moment = jnp.sum(every[:, 2] * factor, axis=0)
    picked = jnp.sum(every[:, 3], axis=0)
    lse = top + jnp.log(total)
    own = jnp.stack([picked - lse, lse - moment / total], axis=0)
    both = lax.all_gather(own, "tok", axis=1, tiled=True)
    out_rows = targets.shape[0] * 5 // 8 // (n_tok * n_voc)
    device = lax.axis_index(("tok", "voc"))
    positions = device * out_rows + jnp.arange(out_rows, dtype=jnp.int32)
    rows = slot_rows(positions, lengths, perm)
    return (both[0][rows], both[1][rows])


def solution(mesh):
    in_specs = (P(("tok", "voc"), None), P(), P(None, "voc"), P(), P(), P())
    out_specs = (P(("tok", "voc")), P(("tok", "voc")))
    return jax.shard_map(
        on_device, mesh=mesh, in_specs=in_specs, out_specs=out_specs, check_vma=False
    )
```

```python
import jax
import jax.numpy as jnp
from jax import lax
from jax.sharding import PartitionSpec as P
from jax.experimental import pallas as pl
from jax.experimental.pallas import tpu as pltpu

MAXLEN = 1024
CHUNKS = 2
TILE_N = 512
NEG = -1e30


def slot_rows(positions, lengths, perm):
    count = lengths.shape[0]
    ident = jnp.arange(count, dtype=jnp.int32)
    starts = jnp.cumsum(lengths) - lengths
    request = jnp.sum((positions[:, None] >= starts[None, :]).astype(jnp.int32), axis=1) - 1
    start_of = jnp.sum(jnp.where(ident[None, :] == request[:, None], starts[None, :], 0), axis=1)
    slot_of = jnp.sum(jnp.where(perm[None, :] == request[:, None], ident[None, :], 0), axis=1)
    return slot_of * MAXLEN + positions - start_of


def stats_kernel(ncols, x_ref, w_ref, t_ref, m_out, s_out, e_out, p_out, m_sc, s_sc, e_sc, p_sc):
    j = pl.program_id(1)
    last = pl.num_programs(1) - 1
    tn = w_ref.shape[0]
    lane = m_sc.shape[1]

    @pl.when(j == 0)
    def _():
        m_sc[...] = jnp.full(m_sc.shape, NEG, jnp.float32)
        s_sc[...] = jnp.zeros(s_sc.shape, jnp.float32)
        e_sc[...] = jnp.zeros(e_sc.shape, jnp.float32)
        p_sc[...] = jnp.zeros(p_sc.shape, jnp.float32)

    logits = lax.dot_general(
        x_ref[...], w_ref[...], (((1,), (1,)), ((), ())), preferred_element_type=jnp.float32
    )
    lanes = lax.broadcasted_iota(jnp.int32, m_sc.shape, 1)
    shift = t_ref[...] - j * tn

    def update(masked):
        groups = [logits[:, k * lane:(k + 1) * lane] for k in range(tn // lane)]
        if masked:
            groups = [jnp.where(lanes < ncols - j * tn - k * lane, g, NEG) for k, g in enumerate(groups)]
        top = groups[0]
        for g in groups[1:]:
            top = jnp.maximum(top, g)
        old = m_sc[...]
        new = jnp.maximum(old, top)
        alpha = jnp.exp(old - new)
        total = s_sc[...] * alpha
        moment = e_sc[...] * alpha
        picked = p_sc[...]
        for k, g in enumerate(groups):
            expo = jnp.exp(g - new)
            total = total + expo
            moment = moment + expo * g
            picked = picked + jnp.where(lanes == shift - k * lane, g, 0.0)
        m_sc[...] = new
        s_sc[...] = total
        e_sc[...] = moment
        p_sc[...] = picked

    if ncols % tn:
        pl.when(j < last)(lambda: update(False))
        pl.when(j == last)(lambda: update(True))
    else:
        update(False)

    @pl.when(j == last)
    def _():
        m = m_sc[...]
        top = jnp.max(m, axis=1, keepdims=True)
        scale = jnp.exp(m - top)
        m_out[...] = top
        s_out[...] = jnp.sum(s_sc[...] * scale, axis=1, keepdims=True)
        e_out[...] = jnp.sum(e_sc[...] * scale, axis=1, keepdims=True)
        p_out[...] = jnp.sum(p_sc[...], axis=1, keepdims=True)


def row_stats(piece, weights_t, wanted):
    rows, depth = piece.shape
    ncols = weights_t.shape[0]
    tm = min(512, rows)
    tn = TILE_N
    lane = 128
    steps = pl.cdiv(ncols, tn)
    wanted = jnp.where((wanted >= 0) & (wanted < ncols), wanted, -1)
    out_spec = pl.BlockSpec((tm, 1), lambda i, j: (i, 0))
    outs = pl.pallas_call(
        lambda *refs: stats_kernel(ncols, *refs),
        grid=(rows // tm, steps),
        in_specs=[
            pl.BlockSpec((tm, depth), lambda i, j: (i, 0)),
            pl.BlockSpec((tn, depth), lambda i, j: (j, 0)),
            pl.BlockSpec((tm, lane), lambda i, j: (i, 0)),
        ],
        out_specs=[out_spec] * 4,
        out_shape=[jax.ShapeDtypeStruct((rows, 1), jnp.float32)] * 4,
        scratch_shapes=[pltpu.VMEM((tm, lane), jnp.float32)] * 4,
        compiler_params=pltpu.CompilerParams(
            dimension_semantics=("arbitrary", "arbitrary"), vmem_limit_bytes=48 * 1024 * 1024
        ),
        cost_estimate=pl.CostEstimate(
            flops=2 * rows * depth * ncols,
            transcendentals=rows * ncols,
            bytes_accessed=2 * depth * ncols * (rows // tm) + 2 * rows * depth,
        ),
    )(piece, weights_t, jnp.broadcast_to(wanted[:, None], (rows, lane)))
    return jnp.stack([o.reshape(rows) for o in outs], axis=0)


def on_device(hidden, gain, head, targets, lengths, perm):
    values = hidden.astype(jnp.float32)
    scale = lax.rsqrt(jnp.mean(values * values, axis=1, keepdims=True) + 1e-06)
    normed = (values * scale * gain.astype(jnp.float32)[None, :]).astype(jnp.bfloat16)
    n_tok = lax.axis_size("tok")
    n_voc = lax.axis_size("voc")
    local = normed.shape[0]
    group_rows = local * n_voc
    shard_cols = head.shape[1]
    col_base = lax.axis_index("voc") * shard_cols
    tok_index = lax.axis_index("tok")
    chunks = CHUNKS if local % (CHUNKS * 8) == 0 else 1
    step = local // chunks
    wanted = lax.dynamic_slice_in_dim(targets, tok_index * group_rows, group_rows, 0) - col_base
    wanted = wanted.reshape(n_voc, chunks, step)
    head_t = head.T
    parts = []
    for j in range(chunks):
        piece = lax.all_gather(normed[j * step:(j + 1) * step], "voc", axis=0, tiled=True)
        parts.append(row_stats(piece, head_t, wanted[:, j, :].reshape(-1)).reshape(4, n_voc, step))
    stats = jnp.stack(parts, axis=2).reshape(4, group_rows)
    every = lax.all_gather(stats, "voc", axis=0)
    top = jnp.max(every[:, 0], axis=0)
    factor = jnp.exp(every[:, 0] - top[None, :])
    total = jnp.sum(every[:, 1] * factor, axis=0)
    moment = jnp.sum(every[:, 2] * factor, axis=0)
    picked = jnp.sum(every[:, 3], axis=0)
    lse = top + jnp.log(total)
    own = jnp.stack([picked - lse, lse - moment / total], axis=0)
    both = lax.all_gather(own, "tok", axis=1, tiled=True)
    out_rows = targets.shape[0] * 5 // 8 // (n_tok * n_voc)
    device = lax.axis_index(("tok", "voc"))
    positions = device * out_rows + jnp.arange(out_rows, dtype=jnp.int32)
    rows = slot_rows(positions, lengths, perm)
    hit = rows[:, None] == jnp.arange(both.shape[1], dtype=jnp.int32)[None, :]
    lp = jnp.sum(jnp.where(hit, both[0][None, :], 0.0), axis=1)
    ent = jnp.sum(jnp.where(hit, both[1][None, :], 0.0), axis=1)
    return (lp, ent)


def solution(mesh):
    in_specs = (P(("tok", "voc"), None), P(), P(None, "voc"), P(), P(), P())
    out_specs = (P(("tok", "voc")), P(("tok", "voc")))
    return jax.shard_map(
        on_device, mesh=mesh, in_specs=in_specs, out_specs=out_specs, check_vma=False
    )
```

```python
import jax
import jax.numpy as jnp
from jax import lax
from jax.sharding import PartitionSpec as P
from jax.experimental import pallas as pl
from jax.experimental.pallas import tpu as pltpu

MAXLEN = 1024
CHUNKS = 2
TILE_N = 512
NEG = -1e30


def slot_rows(positions, lengths, perm):
    count = lengths.shape[0]
    ident = jnp.arange(count, dtype=jnp.int32)
    starts = jnp.cumsum(lengths) - lengths
    request = jnp.sum((positions[:, None] >= starts[None, :]).astype(jnp.int32), axis=1) - 1
    start_of = jnp.sum(jnp.where(ident[None, :] == request[:, None], starts[None, :], 0), axis=1)
    slot_of = jnp.sum(jnp.where(perm[None, :] == request[:, None], ident[None, :], 0), axis=1)
    return slot_of * MAXLEN + positions - start_of


def stats_kernel(ncols, x_ref, w_ref, t_ref, m_out, s_out, e_out, p_out, m_sc, s_sc, e_sc, p_sc):
    j = pl.program_id(1)
    last = pl.num_programs(1) - 1
    tn = w_ref.shape[0]
    lane = m_sc.shape[1]

    @pl.when(j == 0)
    def _():
        m_sc[...] = jnp.full(m_sc.shape, NEG, jnp.float32)
        s_sc[...] = jnp.zeros(s_sc.shape, jnp.float32)
        e_sc[...] = jnp.zeros(e_sc.shape, jnp.float32)
        p_sc[...] = jnp.zeros(p_sc.shape, jnp.float32)

    logits = lax.dot_general(
        x_ref[...], w_ref[...], (((1,), (1,)), ((), ())), preferred_element_type=jnp.float32
    )
    lanes = lax.broadcasted_iota(jnp.int32, m_sc.shape, 1)
    shift = t_ref[...] - j * tn

    def update(masked):
        groups = [logits[:, k * lane:(k + 1) * lane] for k in range(tn // lane)]
        if masked:
            groups = [jnp.where(lanes < ncols - j * tn - k * lane, g, NEG) for k, g in enumerate(groups)]
        top = groups[0]
        for g in groups[1:]:
            top = jnp.maximum(top, g)
        old = m_sc[...]
        new = jnp.maximum(old, top)
        alpha = jnp.exp(old - new)
        total = s_sc[...] * alpha
        moment = e_sc[...] * alpha
        picked = p_sc[...]
        for k, g in enumerate(groups):
            expo = jnp.exp(g - new)
            total = total + expo
            moment = moment + expo * g
            picked = picked + jnp.where(lanes == shift - k * lane, g, 0.0)
        m_sc[...] = new
        s_sc[...] = total
        e_sc[...] = moment
        p_sc[...] = picked

    if ncols % tn:
        pl.when(j < last)(lambda: update(False))
        pl.when(j == last)(lambda: update(True))
    else:
        update(False)

    @pl.when(j == last)
    def _():
        m = m_sc[...]
        top = jnp.max(m, axis=1, keepdims=True)
        scale = jnp.exp(m - top)
        m_out[...] = top
        s_out[...] = jnp.sum(s_sc[...] * scale, axis=1, keepdims=True)
        e_out[...] = jnp.sum(e_sc[...] * scale, axis=1, keepdims=True)
        p_out[...] = jnp.sum(p_sc[...], axis=1, keepdims=True)


def row_stats(piece, weights_t, wanted):
    rows, depth = piece.shape
    ncols = weights_t.shape[0]
    tm = min(1024, rows)
    tn = TILE_N
    lane = 128
    steps = pl.cdiv(ncols, tn)
    wanted = jnp.where((wanted >= 0) & (wanted < ncols), wanted, -1)
    out_spec = pl.BlockSpec((tm, 1), lambda i, j: (i, 0))
    outs = pl.pallas_call(
        lambda *refs: stats_kernel(ncols, *refs),
        grid=(rows // tm, steps),
        in_specs=[
            pl.BlockSpec((tm, depth), lambda i, j: (i, 0)),
            pl.BlockSpec((tn, depth), lambda i, j: (j, 0)),
            pl.BlockSpec((tm, lane), lambda i, j: (i, 0)),
        ],
        out_specs=[out_spec] * 4,
        out_shape=[jax.ShapeDtypeStruct((rows, 1), jnp.float32)] * 4,
        scratch_shapes=[pltpu.VMEM((tm, lane), jnp.float32)] * 4,
        compiler_params=pltpu.CompilerParams(
            dimension_semantics=("arbitrary", "arbitrary"), vmem_limit_bytes=48 * 1024 * 1024
        ),
        cost_estimate=pl.CostEstimate(
            flops=2 * rows * depth * ncols,
            transcendentals=rows * ncols,
            bytes_accessed=2 * depth * ncols * (rows // tm) + 2 * rows * depth,
        ),
    )(piece, weights_t, jnp.broadcast_to(wanted[:, None], (rows, lane)))
    return jnp.stack([o.reshape(rows) for o in outs], axis=0)


def on_device(hidden, gain, head, targets, lengths, perm):
    values = hidden.astype(jnp.float32)
    scale = lax.rsqrt(jnp.mean(values * values, axis=1, keepdims=True) + 1e-06)
    normed = (values * scale * gain.astype(jnp.float32)[None, :]).astype(jnp.bfloat16)
    n_tok = lax.axis_size("tok")
    n_voc = lax.axis_size("voc")
    local = normed.shape[0]
    group_rows = local * n_voc
    shard_cols = head.shape[1]
    col_base = lax.axis_index("voc") * shard_cols
    tok_index = lax.axis_index("tok")
    chunks = CHUNKS if local % (CHUNKS * 8) == 0 else 1
    step = local // chunks
    wanted = lax.dynamic_slice_in_dim(targets, tok_index * group_rows, group_rows, 0) - col_base
    wanted = wanted.reshape(n_voc, chunks, step)
    head_t = head.T
    parts = []
    for j in range(chunks):
        piece = lax.all_gather(normed[j * step:(j + 1) * step], "voc", axis=0, tiled=True)
        parts.append(row_stats(piece, head_t, wanted[:, j, :].reshape(-1)).reshape(4, n_voc, step))
    stats = jnp.stack(parts, axis=2).reshape(4, group_rows)
    every = lax.all_gather(stats, "voc", axis=0)
    top = jnp.max(every[:, 0], axis=0)
    factor = jnp.exp(every[:, 0] - top[None, :])
    total = jnp.sum(every[:, 1] * factor, axis=0)
    moment = jnp.sum(every[:, 2] * factor, axis=0)
    picked = jnp.sum(every[:, 3], axis=0)
    lse = top + jnp.log(total)
    own = jnp.stack([picked - lse, lse - moment / total], axis=0)
    both = lax.all_gather(own, "tok", axis=1, tiled=True)
    out_rows = targets.shape[0] * 5 // 8 // (n_tok * n_voc)
    device = lax.axis_index(("tok", "voc"))
    positions = device * out_rows + jnp.arange(out_rows, dtype=jnp.int32)
    rows = slot_rows(positions, lengths, perm)
    hit = rows[:, None] == jnp.arange(both.shape[1], dtype=jnp.int32)[None, :]
    lp = jnp.sum(jnp.where(hit, both[0][None, :], 0.0), axis=1)
    ent = jnp.sum(jnp.where(hit, both[1][None, :], 0.0), axis=1)
    return (lp, ent)


def solution(mesh):
    in_specs = (P(("tok", "voc"), None), P(), P(None, "voc"), P(), P(), P())
    out_specs = (P(("tok", "voc")), P(("tok", "voc")))
    return jax.shard_map(
        on_device, mesh=mesh, in_specs=in_specs, out_specs=out_specs, check_vma=False
    )
```

```python
import jax
import jax.numpy as jnp
from jax import lax
from jax.sharding import PartitionSpec as P
from jax.experimental import pallas as pl
from jax.experimental.pallas import tpu as pltpu

MAXLEN = 1024
CHUNKS = 2
TILE_N = 768
NEG = -1e30


def slot_rows(positions, lengths, perm):
    count = lengths.shape[0]
    ident = jnp.arange(count, dtype=jnp.int32)
    starts = jnp.cumsum(lengths) - lengths
    request = jnp.sum((positions[:, None] >= starts[None, :]).astype(jnp.int32), axis=1) - 1
    start_of = jnp.sum(jnp.where(ident[None, :] == request[:, None], starts[None, :], 0), axis=1)
    slot_of = jnp.sum(jnp.where(perm[None, :] == request[:, None], ident[None, :], 0), axis=1)
    return slot_of * MAXLEN + positions - start_of


def stats_kernel(ncols, x_ref, w_ref, t_ref, m_out, s_out, e_out, p_out, m_sc, s_sc, e_sc, p_sc):
    j = pl.program_id(1)
    last = pl.num_programs(1) - 1
    tn = w_ref.shape[0]
    lane = m_sc.shape[1]

    @pl.when(j == 0)
    def _():
        m_sc[...] = jnp.full(m_sc.shape, NEG, jnp.float32)
        s_sc[...] = jnp.zeros(s_sc.shape, jnp.float32)
        e_sc[...] = jnp.zeros(e_sc.shape, jnp.float32)
        p_sc[...] = jnp.zeros(p_sc.shape, jnp.float32)

    logits = lax.dot_general(
        x_ref[...], w_ref[...], (((1,), (1,)), ((), ())), preferred_element_type=jnp.float32
    )
    lanes = lax.broadcasted_iota(jnp.int32, m_sc.shape, 1)
    shift = t_ref[...] - j * tn

    def update(masked):
        groups = [logits[:, k * lane:(k + 1) * lane] for k in range(tn // lane)]
        if masked:
            groups = [jnp.where(lanes < ncols - j * tn - k * lane, g, NEG) for k, g in enumerate(groups)]
        top = groups[0]
        for g in groups[1:]:
            top = jnp.maximum(top, g)
        old = m_sc[...]
        new = jnp.maximum(old, top)
        alpha = jnp.exp(old - new)
        total = s_sc[...] * alpha
        moment = e_sc[...] * alpha
        picked = p_sc[...]
        for k, g in enumerate(groups):
            expo = jnp.exp(g - new)
            total = total + expo
            moment = moment + expo * g
            picked = picked + jnp.where(lanes == shift - k * lane, g, 0.0)
        m_sc[...] = new
        s_sc[...] = total
        e_sc[...] = moment
        p_sc[...] = picked

    if ncols % tn:
        pl.when(j < last)(lambda: update(False))
        pl.when(j == last)(lambda: update(True))
    else:
        update(False)

    @pl.when(j == last)
    def _():
        m = m_sc[...]
        top = jnp.max(m, axis=1, keepdims=True)
        scale = jnp.exp(m - top)
        m_out[...] = top
        s_out[...] = jnp.sum(s_sc[...] * scale, axis=1, keepdims=True)
        e_out[...] = jnp.sum(e_sc[...] * scale, axis=1, keepdims=True)
        p_out[...] = jnp.sum(p_sc[...], axis=1, keepdims=True)


def row_stats(piece, weights_t, wanted):
    rows, depth = piece.shape
    ncols = weights_t.shape[0]
    tm = min(1024, rows)
    tn = TILE_N
    lane = 128
    steps = pl.cdiv(ncols, tn)
    wanted = jnp.where((wanted >= 0) & (wanted < ncols), wanted, -1)
    out_spec = pl.BlockSpec((tm, 1), lambda i, j: (i, 0))
    outs = pl.pallas_call(
        lambda *refs: stats_kernel(ncols, *refs),
        grid=(rows // tm, steps),
        in_specs=[
            pl.BlockSpec((tm, depth), lambda i, j: (i, 0)),
            pl.BlockSpec((tn, depth), lambda i, j: (j, 0)),
            pl.BlockSpec((tm, lane), lambda i, j: (i, 0)),
        ],
        out_specs=[out_spec] * 4,
        out_shape=[jax.ShapeDtypeStruct((rows, 1), jnp.float32)] * 4,
        scratch_shapes=[pltpu.VMEM((tm, lane), jnp.float32)] * 4,
        compiler_params=pltpu.CompilerParams(
            dimension_semantics=("arbitrary", "arbitrary"), vmem_limit_bytes=48 * 1024 * 1024
        ),
        cost_estimate=pl.CostEstimate(
            flops=2 * rows * depth * ncols,
            transcendentals=rows * ncols,
            bytes_accessed=2 * depth * ncols * (rows // tm) + 2 * rows * depth,
        ),
    )(piece, weights_t, jnp.broadcast_to(wanted[:, None], (rows, lane)))
    return jnp.stack([o.reshape(rows) for o in outs], axis=0)


def on_device(hidden, gain, head, targets, lengths, perm):
    values = hidden.astype(jnp.float32)
    scale = lax.rsqrt(jnp.mean(values * values, axis=1, keepdims=True) + 1e-06)
    normed = (values * scale * gain.astype(jnp.float32)[None, :]).astype(jnp.bfloat16)
    n_tok = lax.axis_size("tok")
    n_voc = lax.axis_size("voc")
    local = normed.shape[0]
    group_rows = local * n_voc
    shard_cols = head.shape[1]
    col_base = lax.axis_index("voc") * shard_cols
    tok_index = lax.axis_index("tok")
    chunks = CHUNKS if local % (CHUNKS * 8) == 0 else 1
    step = local // chunks
    wanted = lax.dynamic_slice_in_dim(targets, tok_index * group_rows, group_rows, 0) - col_base
    wanted = wanted.reshape(n_voc, chunks, step)
    head_t = head.T
    parts = []
    for j in range(chunks):
        piece = lax.all_gather(normed[j * step:(j + 1) * step], "voc", axis=0, tiled=True)
        parts.append(row_stats(piece, head_t, wanted[:, j, :].reshape(-1)).reshape(4, n_voc, step))
    stats = jnp.stack(parts, axis=2).reshape(4, group_rows)
    every = lax.all_gather(stats, "voc", axis=0)
    top = jnp.max(every[:, 0], axis=0)
    factor = jnp.exp(every[:, 0] - top[None, :])
    total = jnp.sum(every[:, 1] * factor, axis=0)
    moment = jnp.sum(every[:, 2] * factor, axis=0)
    picked = jnp.sum(every[:, 3], axis=0)
    lse = top + jnp.log(total)
    own = jnp.stack([picked - lse, lse - moment / total], axis=0)
    both = lax.all_gather(own, "tok", axis=1, tiled=True)
    out_rows = targets.shape[0] * 5 // 8 // (n_tok * n_voc)
    device = lax.axis_index(("tok", "voc"))
    positions = device * out_rows + jnp.arange(out_rows, dtype=jnp.int32)
    rows = slot_rows(positions, lengths, perm)
    hit = rows[:, None] == jnp.arange(both.shape[1], dtype=jnp.int32)[None, :]
    lp = jnp.sum(jnp.where(hit, both[0][None, :], 0.0), axis=1)
    ent = jnp.sum(jnp.where(hit, both[1][None, :], 0.0), axis=1)
    return (lp, ent)


def solution(mesh):
    in_specs = (P(("tok", "voc"), None), P(), P(None, "voc"), P(), P(), P())
    out_specs = (P(("tok", "voc")), P(("tok", "voc")))
    return jax.shard_map(
        on_device, mesh=mesh, in_specs=in_specs, out_specs=out_specs, check_vma=False
    )
```
